256 devices in a mesh: node: 8 (over y, core), rows: 32 (over z, x).
Axes of the slice: x: 4, y: 4, z: 8, core: 2. Of those that a mesh axis runs over, the one named last changes fastest.
Arguments:
- columns: bfloat16 [32, 768, 128], P(None, 'rows'), may hold values from -6 to 6
- pencil_e: bfloat16 [768, 5, 128, 128], P('rows'), may hold values from -2 to 3, as said below
- pencil_a: bfloat16 [768, 5, 128, 128], P('rows'), may hold values from -5 to 2, as said below
- precond: bfloat16 [8, 2, 768, 128, 128], P('node', None, 'rows'), may hold values from -30 to 30, as said below
- neighbours: int32 [768, 5], P('rows'), may hold values from 0 to 767, as said below
Outputs:
- projected: float32 [2, 32, 768, 128], P(None, 'node', 'rows')
The draws below stay inside these ranges and needn't reach their ends.
Inputs may be any that keep to these rules, and one draw needn't show every extreme that they name: neighbours[i, 0] = i. Every entry lies in the block rows of a device whose index along rows is at most 2 away, or exactly half of the 32 devices away, counted around the cycle. For each device and each other device, at most 6 entries of the first one's block rows lie in the second one's block rows; every device has exactly 6 entries in the block rows of the device half the cycle away. `pencil_e`: slot 0 holds the diagonal block. `pencil_a`: slot 0 holds the diagonal block. precond[k, 0, i] + i precond[k, 1, i] is the inverse of z_k E_i - A_i, where E_i and A_i are the float32 diagonal blocks before they were rounded to give pencil_e[i, 0] and pencil_a[i, 0]; the inverse is then rounded to bfloat16.
All inputs are finite; a program needn't handle non-finite values.
Results may differ from the reference program's by a relative error of at most 0.0017.
Values may be sent and summed in bfloat16 or wider, within the bound.
No kernel may reach another device: no remote copies, remote signals or barrier semaphores. Data moves between devices by JAX's collectives and lax.ppermute only.
A program may use at most 64 MiB of HBM per device.

```python
import math
import jax
import jax.numpy as jnp
from jax import lax

BS = 128
NCOL = 32
SLOTS = 5
RDEV = 24
HMAX = 6
REACH = 2
SWEEPS = 2
NODES = 8
NBT = 768


def pencil_parts(key):
    subkeys = jax.random.split(jax.random.fold_in(key, 11), 3)
    inside = jax.random.uniform(subkeys[0], (NBT,)) < 0.4
    spread = jax.random.uniform(subkeys[1], (NBT,))
    low_band = jnp.exp(jnp.log(0.05) + spread * (jnp.log(0.2) - jnp.log(0.05)))
    high_band = jnp.exp(jnp.log(1.5) + spread * (jnp.log(3.0) - jnp.log(1.5)))
    shifts = jnp.where(inside, low_band, high_band)
    noise = jax.random.normal(subkeys[2], (2, NBT, SLOTS, BS, BS), jnp.float32) / math.sqrt(BS)
    noise = jnp.clip(noise, -6.0 / math.sqrt(BS), 6.0 / math.sqrt(BS))
    diag_slot = (jnp.arange(SLOTS) == 0).astype(jnp.float32)[None, :, None, None]
    scales = 0.1 + 0.02 * diag_slot
    identity = jnp.eye(BS, dtype=jnp.float32)[None, None]
    matrix_e = noise[0] * scales + diag_slot * identity
    matrix_a = noise[1] * scales - diag_slot * identity * shifts[:, None, None, None]
    return (matrix_e, matrix_a)


def draw_pencil_e(key, part):
    return pencil_parts(key)[0].astype(jnp.bfloat16)


def draw_pencil_a(key, part):
    return pencil_parts(key)[1].astype(jnp.bfloat16)


def draw_precond(key, part):
    matrix_e, matrix_a = pencil_parts(key)
    diag_e = matrix_e[:, 0]
    diag_a = matrix_a[:, 0]

    def per_node(node_index):
        angle_node = 2.0 * math.pi * (node_index.astype(jnp.float32) + 0.5) / NODES
        block_real = jnp.cos(angle_node) * diag_e - diag_a
        block_imag = jnp.sin(angle_node) * diag_e
        upper = jnp.concatenate([block_real, block_imag], axis=2)
        lower = jnp.concatenate([-block_imag, block_real], axis=2)
        inverse = jnp.linalg.inv(jnp.concatenate([upper, lower], axis=1))
        return jnp.stack([inverse[:, :BS, :BS], inverse[:, :BS, BS:]])
    return lax.map(per_node, jnp.arange(NODES)).astype(jnp.bfloat16)


def draw_neighbours(key, part):
    devices = NBT // RDEV
    off_count = (SLOTS - 1) * RDEV
    lanes = 2 * REACH + 1
    dev_keys = jax.random.split(jax.random.fold_in(key, 7), devices)

    def one_device(dev_key, device):
        subkeys = jax.random.split(dev_key, 4)
        lane_order = jax.random.permutation(subkeys[0], lanes)
        counts = jax.random.randint(subkeys[1], (lanes,), 0, HMAX + 1)
        counts = jnp.where(lane_order == 2 * REACH, HMAX, counts)
        bounds = jnp.cumsum(counts)
        position = jnp.arange(off_count)
        which = jnp.sum(position[:, None] >= bounds[None, :], axis=1)
        lane_offset = jnp.where(lane_order < REACH, lane_order - REACH, lane_order - REACH + 1)
        lane_offset = jnp.where(lane_order == 2 * REACH, devices // 2, lane_offset)
        chosen = lane_offset[jnp.minimum(which, lanes - 1)]
        chosen = jnp.where(which < lanes, chosen, 0)
        shuffled = jax.random.permutation(subkeys[2], chosen)
        locals_drawn = jax.random.randint(subkeys[3], (off_count,), 0, RDEV)
        owners = (device + shuffled + devices) % devices
        targets = (owners * RDEV + locals_drawn).reshape(RDEV, SLOTS - 1)
        selves = device * RDEV + jnp.arange(RDEV)
        return jnp.concatenate([selves[:, None], targets], axis=1).astype(jnp.int32)
    blocks = jax.vmap(one_device)(dev_keys, jnp.arange(devices))
    return blocks.reshape(NBT, SLOTS)


def block_levels(stream_key, extent, shards, low, top_value):
    factor_of = 1.0
    for dim, blocks in shards:
        draws = jax.random.uniform(jax.random.fold_in(jax.random.fold_in(stream_key, 6), dim), (blocks,), jnp.float32, low / len(shards), top_value / len(shards))
        factor_of = factor_of * jnp.repeat(jnp.exp(draws), extent[dim] // blocks).reshape((-1,) + (1,) * (len(extent) - 1 - dim))
    return factor_of


def centred(stream_key, shape, deviation, reach, cuts=(), kind=jnp.bfloat16):
    result = deviation * jax.random.normal(stream_key, shape, jnp.float32)
    if cuts:
        result = result * block_levels(stream_key, shape, cuts, -0.22, 0.18)
    return jnp.clip(result, -reach, reach).astype(kind)


def setup_inputs(seed: int = 0) -> dict:
    keys = jax.random.split(jax.random.key(seed), 6)
    columns = centred(keys[0], (NCOL, NBT, BS), 1.0, 6.0, ((1, 32),))
    pencil_e = draw_pencil_e(jax.random.fold_in(keys[5], 71), 0)
    pencil_a = draw_pencil_a(jax.random.fold_in(keys[5], 71), 0)
    precond = draw_precond(jax.random.fold_in(keys[5], 71), 0)
    neighbours = draw_neighbours(jax.random.fold_in(keys[5], 71), 0)
    return {"columns": columns, "pencil_e": pencil_e, "pencil_a": pencil_a, "precond": precond, "neighbours": neighbours}


def apply_blocks(vector, matrices, neighbours):
    summed = jnp.zeros(vector.shape, vector.dtype)
    for slot in range(SLOTS):
        picked = vector[:, neighbours[:, slot], :]
        summed = summed + jnp.einsum('cnb,nbd->cnd', picked, matrices[:, slot])
    return summed

def to_half(value):
    return lax.optimization_barrier(value.astype(jnp.bfloat16)).astype(jnp.float32)

def precondition(residual, inverse):
    products = jnp.einsum('pcnb,mnbd->pmcnd', residual, inverse)
    return jnp.stack([products[0, 0] - products[1, 1], products[0, 1] + products[1, 0]])

def reference(columns, pencil_e, pencil_a, precond, neighbours):
    e_full = pencil_e.astype(jnp.float32)
    a_full = pencil_a.astype(jnp.float32)
    rhs_full = apply_blocks(columns.astype(jnp.float32), e_full, neighbours)
    rhs_round = to_half(rhs_full)
    projected = jnp.zeros((2, NCOL, NBT, BS), jnp.float32)
    for node_index in range(NODES):
        angle_node = 2.0 * math.pi * (node_index + 0.5) / NODES
        node_real = math.cos(angle_node)
        node_imag = math.sin(angle_node)
        inverse = precond[node_index].astype(jnp.float32)
        iterate = jnp.einsum('cnb,mnbd->mcnd', rhs_round, inverse)
        for sweep_step in range(SWEEPS):
            rounded = to_half(iterate).reshape(2 * NCOL, NBT, BS)
            with_e = apply_blocks(rounded, e_full, neighbours).reshape(2, NCOL, NBT, BS)
            with_a = apply_blocks(rounded, a_full, neighbours).reshape(2, NCOL, NBT, BS)
            applied_real = node_real * with_e[0] - node_imag * with_e[1] - with_a[0]
            applied_imag = node_real * with_e[1] + node_imag * with_e[0] - with_a[1]
            residual = to_half(jnp.stack([rhs_full - applied_real, -applied_imag]))
            iterate = iterate + precondition(residual, inverse)
        weighted = jnp.stack([node_real * iterate[0] - node_imag * iterate[1], node_real * iterate[1] + node_imag * iterate[0]])
        projected = projected + weighted / NODES
    return projected
```

```python
import math

import jax
import jax.numpy as jnp
from jax import lax
from jax.sharding import PartitionSpec as P

SLOTS = 5
HMAX = 6
REACH = 2
SWEEPS = 2


def partner_offsets(peer_count):
    found = []
    for offset in list(range(1, REACH + 1)) + [peer_count // 2] + [-o for o in range(1, REACH + 1)]:
        offset = offset % peer_count
        if offset != 0 and offset not in found:
            found.append(offset)
    return found


def apply_pair(extended, slot_index, first, second):
    picked = extended[slot_index]
    with_first = jnp.einsum("nscb,nsbd->ncd", picked, first, preferred_element_type=jnp.float32)
    if second is None:
        return with_first, None
    with_second = jnp.einsum("nscb,nsbd->ncd", picked, second, preferred_element_type=jnp.float32)
    return with_first, with_second


def per_device(columns, pencil_e, pencil_a, precond, neighbours):
    dev_rows = pencil_e.shape[0]
    col_count = columns.shape[0]
    peer_count = lax.axis_size("rows")
    my_index = lax.axis_index("rows")
    offsets = partner_offsets(peer_count)
    owners = neighbours // dev_rows
    local_ids = neighbours - owners * dev_rows
    relative = (owners - my_index) % peer_count
    flat_rel = relative.reshape(-1)
    flat_local = local_ids.reshape(-1)
    slot_flat = flat_local
    wanted = []
    rank_range = jnp.arange(HMAX)
    for which, offset in enumerate(offsets):
        hit = flat_rel == offset
        rank = jnp.cumsum(hit.astype(jnp.int32)) - 1
        slot_flat = jnp.where(hit, dev_rows + which * HMAX + rank, slot_flat)
        matched = hit[None, :] & (rank[None, :] == rank_range[:, None])
        wanted.append(jnp.sum(jnp.where(matched, flat_local[None, :], 0), axis=1))
    slot_index = slot_flat.reshape(dev_rows, SLOTS)

    def to_partner(offset):
        return [(j, (j + offset) % peer_count) for j in range(peer_count)]

    def from_partner(offset):
        return [((j + offset) % peer_count, j) for j in range(peer_count)]

    asked_for = [
        lax.ppermute(wanted[which], "rows", to_partner(offset)) for which, offset in enumerate(offsets)
    ]

    def fetch_halo(vector):
        pieces = [vector]
        for which, offset in enumerate(offsets):
            pieces.append(lax.ppermute(vector[asked_for[which]], "rows", from_partner(offset)))
        return jnp.concatenate(pieces, axis=0)

    e_mats = pencil_e
    a_mats = pencil_a
    cols_major = jnp.transpose(columns, (1, 0, 2))
    rhs_full, _ = apply_pair(fetch_halo(cols_major), slot_index, e_mats, None)
    node_count = lax.axis_size("node")
    angle_node = 2.0 * math.pi * (lax.axis_index("node").astype(jnp.float32) + 0.5) / node_count
    node_real = jnp.cos(angle_node)
    node_imag = jnp.sin(angle_node)
    inverse = precond[0]
    rhs_round = rhs_full.astype(jnp.bfloat16)
    start = jnp.einsum("ncb,mnbd->nmcd", rhs_round, inverse, preferred_element_type=jnp.float32)
    iterate = start.reshape(dev_rows, 2 * col_count, -1)
    for sweep_step in range(SWEEPS):
        rounded = iterate.astype(jnp.bfloat16)
        with_e, with_a = apply_pair(fetch_halo(rounded), slot_index, e_mats, a_mats)
        e_real, e_imag = with_e[:, :col_count], with_e[:, col_count:]
        applied_real = node_real * e_real - node_imag * e_imag - with_a[:, :col_count]
        applied_imag = node_real * e_imag + node_imag * e_real - with_a[:, col_count:]
        residual = jnp.concatenate([rhs_full - applied_real, -applied_imag], axis=1).astype(jnp.bfloat16)
        products = jnp.einsum("ncb,mnbd->nmcd", residual, inverse, preferred_element_type=jnp.float32)
        products = products.reshape(dev_rows, 2, 2, col_count, -1)
        update_real = products[:, 0, 0] - products[:, 1, 1]
        update_imag = products[:, 1, 0] + products[:, 0, 1]
        iterate = iterate + jnp.concatenate([update_real, update_imag], axis=1)
    it_real, it_imag = iterate[:, :col_count], iterate[:, col_count:]
    weighted = jnp.stack(
        [
            node_real * it_real - node_imag * it_imag,
            node_real * it_imag + node_imag * it_real,
        ]
    )
    weighted = jnp.transpose(weighted / node_count, (0, 2, 1, 3))
    return lax.psum_scatter(weighted, "node", scatter_dimension=1, tiled=True)


def solution(mesh):
    placed = (
        P(None, "rows", None),
        P("rows", None, None, None),
        P("rows", None, None, None),
        P("node", None, "rows", None, None),
        P("rows", None),
    )
    return jax.shard_map(
        per_device,
        mesh=mesh,
        in_specs=placed,
        out_specs=P(None, "node", "rows", None),
        check_vma=False,
    )
```

```python
import math

import jax
import jax.numpy as jnp
from jax import lax
from jax.sharding import PartitionSpec as P

SLOTS = 5
HMAX = 6
REACH = 2
SWEEPS = 2


def partner_offsets(peer_count):
    found = []
    for offset in list(range(1, REACH + 1)) + [peer_count // 2] + [-o for o in range(1, REACH + 1)]:
        offset = offset % peer_count
        if offset != 0 and offset not in found:
            found.append(offset)
    return found


def apply_pair(extended, slot_index, first, second):
    picked = extended[slot_index]
    with_first = jnp.einsum("nscb,nsbd->ncd", picked, first, preferred_element_type=jnp.float32)
    if second is None:
        return with_first, None
    with_second = jnp.einsum("nscb,nsbd->ncd", picked, second, preferred_element_type=jnp.float32)
    return with_first, with_second


def per_device(columns, pencil_e, pencil_a, precond, neighbours):
    dev_rows = pencil_e.shape[0]
    col_count = columns.shape[0]
    peer_count = lax.axis_size("rows")
    my_index = lax.axis_index("rows")
    offsets = partner_offsets(peer_count)
    owners = neighbours // dev_rows
    local_ids = neighbours - owners * dev_rows
    relative = (owners - my_index) % peer_count
    flat_rel = relative.reshape(-1)
    flat_local = local_ids.reshape(-1)
    slot_flat = flat_local
    wanted = []
    rank_range = jnp.arange(HMAX)
    for which, offset in enumerate(offsets):
        hit = flat_rel == offset
        rank = jnp.cumsum(hit.astype(jnp.int32)) - 1
        slot_flat = jnp.where(hit, dev_rows + which * HMAX + rank, slot_flat)
        matched = hit[None, :] & (rank[None, :] == rank_range[:, None])
        wanted.append(jnp.sum(jnp.where(matched, flat_local[None, :], 0), axis=1))
    slot_index = slot_flat.reshape(dev_rows, SLOTS)

    def to_partner(offset):
        return [(j, (j + offset) % peer_count) for j in range(peer_count)]

    def from_partner(offset):
        return [((j + offset) % peer_count, j) for j in range(peer_count)]

    asked_for = [
        lax.ppermute(wanted[which], "rows", to_partner(offset)) for which, offset in enumerate(offsets)
    ]

    def fetch_halo(vector):
        pieces = [vector]
        for which, offset in enumerate(offsets):
            pieces.append(lax.ppermute(vector[asked_for[which]], "rows", from_partner(offset)))
        return jnp.concatenate(pieces, axis=0)

    e_mats = pencil_e
    a_mats = pencil_a
    cols_major = jnp.transpose(columns, (1, 0, 2))
    rhs_full, _ = apply_pair(fetch_halo(cols_major), slot_index, e_mats, None)
    node_count = lax.axis_size("node")
    angle_node = 2.0 * math.pi * (lax.axis_index("node").astype(jnp.float32) + 0.5) / node_count
    node_real = jnp.cos(angle_node)
    node_imag = jnp.sin(angle_node)
    inverse = precond[0]
    rhs_round = rhs_full.astype(jnp.bfloat16)
    start = jnp.einsum("ncb,mnbd->nmcd", rhs_round, inverse, preferred_element_type=jnp.float32)
    iterate = start.reshape(dev_rows, 2 * col_count, -1)
    for sweep_step in range(SWEEPS):
        rounded = iterate.astype(jnp.bfloat16)
        with_e, with_a = apply_pair(fetch_halo(rounded), slot_index, e_mats, a_mats)
        e_real, e_imag = with_e[:, :col_count], with_e[:, col_count:]
        applied_real = node_real * e_real - node_imag * e_imag - with_a[:, :col_count]
        applied_imag = node_real * e_imag + node_imag * e_real - with_a[:, col_count:]
        residual = jnp.concatenate([rhs_full - applied_real, -applied_imag], axis=1).astype(jnp.bfloat16)
        products = jnp.einsum("ncb,mnbd->nmcd", residual, inverse, preferred_element_type=jnp.float32)
        products = products.reshape(dev_rows, 2, 2, col_count, -1)
        update_real = products[:, 0, 0] - products[:, 1, 1]
        update_imag = products[:, 1, 0] + products[:, 0, 1]
        iterate = iterate + jnp.concatenate([update_real, update_imag], axis=1)
    node_index = lax.axis_index("node")
    parts = iterate.reshape(dev_rows, 2, node_count, col_count // node_count, -1)
    it_real, it_imag = parts[:, 0], parts[:, 1]
    weighted = jnp.stack(
        [
            node_real * it_real - node_imag * it_imag,
            node_real * it_imag + node_imag * it_real,
        ]
    )
    weighted = jnp.transpose(weighted / node_count, (2, 0, 3, 1, 4))
    total = lax.dynamic_index_in_dim(weighted, node_index, 0, keepdims=False)
    for offset in range(1, node_count):
        chunk = lax.dynamic_index_in_dim(weighted, (node_index + offset) % node_count, 0, keepdims=False)
        perm = [(j, (j + offset) % node_count) for j in range(node_count)]
        total = total + lax.ppermute(chunk, "node", perm)
    return total


def solution(mesh):
    placed = (
        P(None, "rows", None),
        P("rows", None, None, None),
        P("rows", None, None, None),
        P("node", None, "rows", None, None),
        P("rows", None),
    )
    return jax.shard_map(
        per_device,
        mesh=mesh,
        in_specs=placed,
        out_specs=P(None, "node", "rows", None),
        check_vma=False,
    )
```

```python
import math

import jax
import jax.numpy as jnp
from jax import lax
from jax.sharding import PartitionSpec as P

SLOTS = 5
HMAX = 6
REACH = 2
SWEEPS = 2


def partner_offsets(peer_count):
    found = []
    for offset in list(range(1, REACH + 1)) + [peer_count // 2] + [-o for o in range(1, REACH + 1)]:
        offset = offset % peer_count
        if offset != 0 and offset not in found:
            found.append(offset)
    return found


def apply_pair(extended, slot_index, first, second):
    picked = extended[slot_index]
    with_first = jnp.einsum("nscb,nsbd->ncd", picked, first, preferred_element_type=jnp.float32)
    if second is None:
        return with_first, None
    with_second = jnp.einsum("nscb,nsbd->ncd", picked, second, preferred_element_type=jnp.float32)
    return with_first, with_second


def per_device(columns, pencil_e, pencil_a, precond, neighbours):
    dev_rows = pencil_e.shape[0]
    col_count = columns.shape[0]
    peer_count = lax.axis_size("rows")
    my_index = lax.axis_index("rows")
    offsets = partner_offsets(peer_count)
    owners = neighbours // dev_rows
    local_ids = neighbours - owners * dev_rows
    relative = (owners - my_index) % peer_count
    flat_rel = relative.reshape(-1)
    flat_local = local_ids.reshape(-1)
    slot_flat = flat_local
    whole_flat = flat_local
    wanted = []
    rank_range = jnp.arange(HMAX)
    for which, offset in enumerate(offsets):
        hit = flat_rel == offset
        rank = jnp.cumsum(hit.astype(jnp.int32)) - 1
        slot_flat = jnp.where(hit, dev_rows + which * HMAX + rank, slot_flat)
        whole_flat = jnp.where(hit, (which + 1) * dev_rows + flat_local, whole_flat)
        matched = hit[None, :] & (rank[None, :] == rank_range[:, None])
        wanted.append(jnp.sum(jnp.where(matched, flat_local[None, :], 0), axis=1))
    slot_index = slot_flat.reshape(dev_rows, SLOTS)
    whole_index = whole_flat.reshape(dev_rows, SLOTS)

    def to_partner(offset):
        return [(j, (j + offset) % peer_count) for j in range(peer_count)]

    def from_partner(offset):
        return [((j + offset) % peer_count, j) for j in range(peer_count)]

    asked_for = [
        lax.ppermute(wanted[which], "rows", to_partner(offset)) for which, offset in enumerate(offsets)
    ]

    def fetch_halo(vector):
        pieces = [vector]
        for which, offset in enumerate(offsets):
            pieces.append(lax.ppermute(vector[asked_for[which]], "rows", from_partner(offset)))
        return jnp.concatenate(pieces, axis=0)

    e_mats = pencil_e
    a_mats = pencil_a
    cols_major = jnp.transpose(columns, (1, 0, 2))
    whole = [cols_major] + [lax.ppermute(cols_major, "rows", from_partner(offset)) for offset in offsets]
    rhs_full, _ = apply_pair(jnp.concatenate(whole, axis=0), whole_index, e_mats, None)
    node_count = lax.axis_size("node")
    angle_node = 2.0 * math.pi * (lax.axis_index("node").astype(jnp.float32) + 0.5) / node_count
    node_real = jnp.cos(angle_node)
    node_imag = jnp.sin(angle_node)
    inverse = precond[0]
    rhs_round = rhs_full.astype(jnp.bfloat16)
    start = jnp.einsum("ncb,mnbd->nmcd", rhs_round, inverse, preferred_element_type=jnp.float32)
    iterate = start.reshape(dev_rows, 2 * col_count, -1)
    for sweep_step in range(SWEEPS):
        rounded = iterate.astype(jnp.bfloat16)
        with_e, with_a = apply_pair(fetch_halo(rounded), slot_index, e_mats, a_mats)
        e_real, e_imag = with_e[:, :col_count], with_e[:, col_count:]
        applied_real = node_real * e_real - node_imag * e_imag - with_a[:, :col_count]
        applied_imag = node_real * e_imag + node_imag * e_real - with_a[:, col_count:]
        residual = jnp.concatenate([rhs_full - applied_real, -applied_imag], axis=1).astype(jnp.bfloat16)
        products = jnp.einsum("ncb,mnbd->nmcd", residual, inverse, preferred_element_type=jnp.float32)
        products = products.reshape(dev_rows, 2, 2, col_count, -1)
        update_real = products[:, 0, 0] - products[:, 1, 1]
        update_imag = products[:, 1, 0] + products[:, 0, 1]
        iterate = iterate + jnp.concatenate([update_real, update_imag], axis=1)
    node_index = lax.axis_index("node")
    parts = iterate.reshape(dev_rows, 2, node_count, col_count // node_count, -1)
    it_real, it_imag = parts[:, 0], parts[:, 1]
    weighted = jnp.stack(
        [
            node_real * it_real - node_imag * it_imag,
            node_real * it_imag + node_imag * it_real,
        ]
    )
    weighted = jnp.transpose(weighted / node_count, (2, 0, 3, 1, 4))
    total = lax.dynamic_index_in_dim(weighted, node_index, 0, keepdims=False)
    for offset in range(1, node_count):
        chunk = lax.dynamic_index_in_dim(weighted, (node_index + offset) % node_count, 0, keepdims=False)
        perm = [(j, (j + offset) % node_count) for j in range(node_count)]
        total = total + lax.ppermute(chunk, "node", perm)
    return total


def solution(mesh):
    placed = (
        P(None, "rows", None),
        P("rows", None, None, None),
        P("rows", None, None, None),
        P("node", None, "rows", None, None),
        P("rows", None),
    )
    return jax.shard_map(
        per_device,
        mesh=mesh,
        in_specs=placed,
        out_specs=P(None, "node", "rows", None),
        check_vma=False,
    )
```

```python
import math

import jax
import jax.numpy as jnp
from jax import lax
from jax.sharding import PartitionSpec as P

SLOTS = 5
HMAX = 6
REACH = 2
SWEEPS = 2


def partner_offsets(peer_count):
    found = []
    for offset in list(range(1, REACH + 1)) + [peer_count // 2] + [-o for o in range(1, REACH + 1)]:
        offset = offset % peer_count
        if offset != 0 and offset not in found:
            found.append(offset)
    return found


def apply_pair(extended, slot_index, first, second):
    picked = extended[slot_index]
    with_first = jnp.einsum("nscb,nsbd->ncd", picked, first, preferred_element_type=jnp.float32)
    if second is None:
        return with_first, None
    with_second = jnp.einsum("nscb,nsbd->ncd", picked, second, preferred_element_type=jnp.float32)
    return with_first, with_second


def per_device(columns, pencil_e, pencil_a, precond, neighbours):
    dev_rows = pencil_e.shape[0]
    col_count = columns.shape[0]
    peer_count = lax.axis_size("rows")
    my_index = lax.axis_index("rows")
    offsets = partner_offsets(peer_count)
    owners = neighbours // dev_rows
    local_ids = neighbours - owners * dev_rows
    relative = (owners - my_index) % peer_count
    flat_rel = relative.reshape(-1)
    flat_local = local_ids.reshape(-1)
    slot_flat = flat_local
    whole_flat = flat_local
    wanted = []
    rank_range = jnp.arange(HMAX)
    for which, offset in enumerate(offsets):
        hit = flat_rel == offset
        rank = jnp.cumsum(hit.astype(jnp.int32)) - 1
        slot_flat = jnp.where(hit, dev_rows + which * HMAX + rank, slot_flat)
        whole_flat = jnp.where(hit, (which + 1) * dev_rows + flat_local, whole_flat)
        matched = hit[None, :] & (rank[None, :] == rank_range[:, None])
        wanted.append(jnp.sum(jnp.where(matched, flat_local[None, :], 0), axis=1))
    slot_index = slot_flat.reshape(dev_rows, SLOTS)
    whole_index = whole_flat.reshape(dev_rows, SLOTS)

    def to_partner(offset):
        return [(j, (j + offset) % peer_count) for j in range(peer_count)]

    def from_partner(offset):
        return [((j + offset) % peer_count, j) for j in range(peer_count)]

    def fetch_halo(vector):
        pieces = [vector]
        for which, offset in enumerate(offsets):
            pieces.append(lax.ppermute(vector[asked_for[which]], "rows", from_partner(offset)))
        return jnp.concatenate(pieces, axis=0)

    e_mats = pencil_e
    a_mats = pencil_a
    cols_major = jnp.transpose(columns, (1, 0, 2))
    whole = [cols_major]
    asked_for = [None] * len(offsets)
    for which, offset in enumerate(offsets):
        back = offsets.index((-offset) % peer_count)
        tag = jnp.zeros((1,) + cols_major.shape[1:], cols_major.dtype)
        tag = tag.at[0, 0, :HMAX].set(wanted[back].astype(cols_major.dtype))
        got = lax.ppermute(jnp.concatenate([cols_major, tag], axis=0), "rows", from_partner(offset))
        whole.append(got[:dev_rows])
        asked_for[back] = got[dev_rows, 0, :HMAX].astype(jnp.int32)
    rhs_full, _ = apply_pair(jnp.concatenate(whole, axis=0), whole_index, e_mats, None)
    node_count = lax.axis_size("node")
    angle_node = 2.0 * math.pi * (lax.axis_index("node").astype(jnp.float32) + 0.5) / node_count
    node_real = jnp.cos(angle_node)
    node_imag = jnp.sin(angle_node)
    inverse = precond[0]
    rhs_round = rhs_full.astype(jnp.bfloat16)
    start = jnp.einsum("ncb,mnbd->nmcd", rhs_round, inverse, preferred_element_type=jnp.float32)
    iterate = start.reshape(dev_rows, 2 * col_count, -1)
    for sweep_step in range(SWEEPS):
        rounded = iterate.astype(jnp.bfloat16)
        with_e, with_a = apply_pair(fetch_halo(rounded), slot_index, e_mats, a_mats)
        e_real, e_imag = with_e[:, :col_count], with_e[:, col_count:]
        applied_real = node_real * e_real - node_imag * e_imag - with_a[:, :col_count]
        applied_imag = node_real * e_imag + node_imag * e_real - with_a[:, col_count:]
        residual = jnp.concatenate([rhs_full - applied_real, -applied_imag], axis=1).astype(jnp.bfloat16)
        products = jnp.einsum("ncb,mnbd->nmcd", residual, inverse, preferred_element_type=jnp.float32)
        products = products.reshape(dev_rows, 2, 2, col_count, -1)
        update_real = products[:, 0, 0] - products[:, 1, 1]
        update_imag = products[:, 1, 0] + products[:, 0, 1]
        iterate = iterate + jnp.concatenate([update_real, update_imag], axis=1)
    node_index = lax.axis_index("node")
    parts = iterate.reshape(dev_rows, 2, node_count, col_count // node_count, -1)
    it_real, it_imag = parts[:, 0], parts[:, 1]
    weighted = jnp.stack(
        [
            node_real * it_real - node_imag * it_imag,
            node_real * it_imag + node_imag * it_real,
        ]
    )
    weighted = jnp.transpose(weighted / node_count, (2, 0, 3, 1, 4))
    total = lax.dynamic_index_in_dim(weighted, node_index, 0, keepdims=False)
    for offset in range(1, node_count):
        chunk = lax.dynamic_index_in_dim(weighted, (node_index + offset) % node_count, 0, keepdims=False)
        perm = [(j, (j + offset) % node_count) for j in range(node_count)]
        total = total + lax.ppermute(chunk, "node", perm)
    return total


def solution(mesh):
    placed = (
        P(None, "rows", None),
        P("rows", None, None, None),
        P("rows", None, None, None),
        P("node", None, "rows", None, None),
        P("rows", None),
    )
    return jax.shard_map(
        per_device,
        mesh=mesh,
        in_specs=placed,
        out_specs=P(None, "node", "rows", None),
        check_vma=False,
    )
```

```python
import math

import jax
import jax.numpy as jnp
from jax import lax
from jax.sharding import PartitionSpec as P

SLOTS = 5
HMAX = 6
REACH = 2
SWEEPS = 2


def partner_offsets(peer_count):
    found = []
    for offset in list(range(1, REACH + 1)) + [peer_count // 2] + [-o for o in range(1, REACH + 1)]:
        offset = offset % peer_count
        if offset != 0 and offset not in found:
            found.append(offset)
    return found


def apply_split(local_vec, halo_vec, local_index, halo_row, mats, halo_mats):
    padded = jnp.concatenate([local_vec, jnp.zeros((1,) + local_vec.shape[1:], local_vec.dtype)], axis=0)
    picked = padded[local_index]
    rows = local_vec.shape[0]
    results = []
    for matrices, halo_matrices in zip(mats, halo_mats):
        summed = jnp.einsum("nscb,nsbd->ncd", picked, matrices, preferred_element_type=jnp.float32)
        extra = jnp.einsum("hcb,hbd->hcd", halo_vec, halo_matrices, preferred_element_type=jnp.float32)
        extra = jnp.zeros((rows + 1,) + extra.shape[1:], jnp.float32).at[halo_row].add(extra)
        results.append(summed + extra[:rows])
    return results


def per_device(columns, pencil_e, pencil_a, precond, neighbours):
    dev_rows = pencil_e.shape[0]
    col_count = columns.shape[0]
    peer_count = lax.axis_size("rows")
    my_index = lax.axis_index("rows")
    offsets = partner_offsets(peer_count)
    owners = neighbours // dev_rows
    local_ids = neighbours - owners * dev_rows
    relative = (owners - my_index) % peer_count
    flat_rel = relative.reshape(-1)
    flat_local = local_ids.reshape(-1)
    entries = flat_local.shape[0]
    local_flat = jnp.where(flat_rel == 0, flat_local, dev_rows)
    wanted = []
    halo_entry = []
    halo_valid = []
    rank_range = jnp.arange(HMAX)
    entry_range = jnp.arange(entries)
    for which, offset in enumerate(offsets):
        hit = flat_rel == offset
        rank = jnp.cumsum(hit.astype(jnp.int32)) - 1
        matched = hit[None, :] & (rank[None, :] == rank_range[:, None])
        wanted.append(jnp.sum(jnp.where(matched, flat_local[None, :], 0), axis=1))
        halo_entry.append(jnp.sum(jnp.where(matched, entry_range[None, :], 0), axis=1))
        halo_valid.append(jnp.any(matched, axis=1))
    local_index = local_flat.reshape(dev_rows, SLOTS)
    halo_entry = jnp.concatenate(halo_entry)
    halo_valid = jnp.concatenate(halo_valid)
    halo_row = jnp.where(halo_valid, halo_entry // SLOTS, dev_rows)

    def to_partner(offset):
        return [(j, (j + offset) % peer_count) for j in range(peer_count)]

    def from_partner(offset):
        return [((j + offset) % peer_count, j) for j in range(peer_count)]

    def fetch_halo(vector):
        pieces = []
        for which, offset in enumerate(offsets):
            pieces.append(lax.ppermute(vector[asked_for[which]], "rows", from_partner(offset)))
        return jnp.concatenate(pieces, axis=0)

    e_mats = pencil_e
    a_mats = pencil_a
    block_shape = pencil_e.shape[2:]
    halo_e = pencil_e.reshape((-1,) + block_shape)[halo_entry]
    halo_a = pencil_a.reshape((-1,) + block_shape)[halo_entry]
    halo_e = jnp.where(halo_valid[:, None, None], halo_e, jnp.zeros_like(halo_e))
    halo_a = jnp.where(halo_valid[:, None, None], halo_a, jnp.zeros_like(halo_a))
    cols_major = jnp.transpose(columns, (1, 0, 2))
    col_halo = []
    asked_for = [None] * len(offsets)
    for which, offset in enumerate(offsets):
        back = offsets.index((-offset) % peer_count)
        tag = jnp.zeros((1,) + cols_major.shape[1:], cols_major.dtype)
        tag = tag.at[0, 0, :HMAX].set(wanted[back].astype(cols_major.dtype))
        got = lax.ppermute(jnp.concatenate([cols_major, tag], axis=0), "rows", from_partner(offset))
        col_halo.append(got[:dev_rows][wanted[which]])
        asked_for[back] = got[dev_rows, 0, :HMAX].astype(jnp.int32)
    col_halo = jnp.concatenate(col_halo, axis=0)
    (rhs_full,) = apply_split(cols_major, col_halo, local_index, halo_row, [e_mats], [halo_e])
    node_count = lax.axis_size("node")
    angle_node = 2.0 * math.pi * (lax.axis_index("node").astype(jnp.float32) + 0.5) / node_count
    node_real = jnp.cos(angle_node)
    node_imag = jnp.sin(angle_node)
    inverse = precond[0]
    rhs_round = rhs_full.astype(jnp.bfloat16)
    start = jnp.einsum("ncb,mnbd->nmcd", rhs_round, inverse, preferred_element_type=jnp.float32)
    iterate = start.reshape(dev_rows, 2 * col_count, -1)
    for sweep_step in range(SWEEPS):
        rounded = iterate.astype(jnp.bfloat16)
        with_e, with_a = apply_split(
            rounded, fetch_halo(rounded), local_index, halo_row, [e_mats, a_mats], [halo_e, halo_a]
        )
        e_real, e_imag = with_e[:, :col_count], with_e[:, col_count:]
        applied_real = node_real * e_real - node_imag * e_imag - with_a[:, :col_count]
        applied_imag = node_real * e_imag + node_imag * e_real - with_a[:, col_count:]
        residual = jnp.concatenate([rhs_full - applied_real, -applied_imag], axis=1).astype(jnp.bfloat16)
        products = jnp.einsum("ncb,mnbd->nmcd", residual, inverse, preferred_element_type=jnp.float32)
        products = products.reshape(dev_rows, 2, 2, col_count, -1)
        update_real = products[:, 0, 0] - products[:, 1, 1]
        update_imag = products[:, 1, 0] + products[:, 0, 1]
        iterate = iterate + jnp.concatenate([update_real, update_imag], axis=1)
    node_index = lax.axis_index("node")
    parts = iterate.reshape(dev_rows, 2, node_count, col_count // node_count, -1)
    it_real, it_imag = parts[:, 0], parts[:, 1]
    weighted = jnp.stack(
        [
            node_real * it_real - node_imag * it_imag,
            node_real * it_imag + node_imag * it_real,
        ]
    )
    weighted = jnp.transpose(weighted / node_count, (2, 0, 3, 1, 4))
    total = lax.dynamic_index_in_dim(weighted, node_index, 0, keepdims=False)
    for offset in range(1, node_count):
        chunk = lax.dynamic_index_in_dim(weighted, (node_index + offset) % node_count, 0, keepdims=False)
        perm = [(j, (j + offset) % node_count) for j in range(node_count)]
        total = total + lax.ppermute(chunk, "node", perm)
    return total


def solution(mesh):
    placed = (
        P(None, "rows", None),
        P("rows", None, None, None),
        P("rows", None, None, None),
        P("node", None, "rows", None, None),
        P("rows", None),
    )
    return jax.shard_map(
        per_device,
        mesh=mesh,
        in_specs=placed,
        out_specs=P(None, "node", "rows", None),
        check_vma=False,
    )
```

```python
import math

import jax
import jax.numpy as jnp
from jax import lax
from jax.sharding import PartitionSpec as P

SLOTS = 5
HMAX = 6
REACH = 2
SWEEPS = 2


def partner_offsets(peer_count):
    found = []
    for offset in list(range(1, REACH + 1)) + [peer_count // 2] + [-o for o in range(1, REACH + 1)]:
        offset = offset % peer_count
        if offset != 0 and offset not in found:
            found.append(offset)
    return found


def apply_pair(extended, slot_index, first, second):
    picked = extended[slot_index]
    with_first = jnp.einsum("nscb,nsbd->ncd", picked, first, preferred_element_type=jnp.float32)
    if second is None:
        return with_first, None
    with_second = jnp.einsum("nscb,nsbd->ncd", picked, second, preferred_element_type=jnp.float32)
    return with_first, with_second


def per_device(columns, pencil_e, pencil_a, precond, neighbours):
    dev_rows = pencil_e.shape[0]
    col_count = columns.shape[0]
    peer_count = lax.axis_size("rows")
    my_index = lax.axis_index("rows")
    offsets = partner_offsets(peer_count)
    owners = neighbours // dev_rows
    local_ids = neighbours - owners * dev_rows
    relative = (owners - my_index) % peer_count
    flat_rel = relative.reshape(-1)
    flat_local = local_ids.reshape(-1)
    slot_flat = flat_local
    whole_flat = flat_local
    wanted = []
    rank_range = jnp.arange(HMAX)
    for which, offset in enumerate(offsets):
        hit = flat_rel == offset
        rank = jnp.cumsum(hit.astype(jnp.int32)) - 1
        slot_flat = jnp.where(hit, dev_rows + which * HMAX + rank, slot_flat)
        whole_flat = jnp.where(hit, (which + 1) * dev_rows + flat_local, whole_flat)
        matched = hit[None, :] & (rank[None, :] == rank_range[:, None])
        wanted.append(jnp.sum(jnp.where(matched, flat_local[None, :], 0), axis=1))
    slot_index = slot_flat.reshape(dev_rows, SLOTS)
    whole_index = whole_flat.reshape(dev_rows, SLOTS)

    def to_partner(offset):
        return [(j, (j + offset) % peer_count) for j in range(peer_count)]

    def from_partner(offset):
        return [((j + offset) % peer_count, j) for j in range(peer_count)]

    def fetch_halo(vector):
        pieces = [vector]
        for which, offset in enumerate(offsets):
            pieces.append(lax.ppermute(vector[asked_for[which]], "rows", from_partner(offset)))
        return jnp.concatenate(pieces, axis=0)

    e_mats = pencil_e
    a_mats = pencil_a
    cols_major = jnp.transpose(columns, (1, 0, 2))
    whole = [cols_major]
    asked_for = [None] * len(offsets)
    for which, offset in enumerate(offsets):
        back = offsets.index((-offset) % peer_count)
        tag = jnp.zeros((1,) + cols_major.shape[1:], cols_major.dtype)
        tag = tag.at[0, 0, :HMAX].set(wanted[back].astype(cols_major.dtype))
        got = lax.ppermute(jnp.concatenate([cols_major, tag], axis=0), "rows", from_partner(offset))
        whole.append(got[:dev_rows])
        asked_for[back] = got[dev_rows, 0, :HMAX].astype(jnp.int32)
    rhs_full, _ = apply_pair(jnp.concatenate(whole, axis=0), whole_index, e_mats, None)
    node_count = lax.axis_size("node")
    angle_node = 2.0 * math.pi * (lax.axis_index("node").astype(jnp.float32) + 0.5) / node_count
    node_real = jnp.cos(angle_node)
    node_imag = jnp.sin(angle_node)
    inverse = precond[0]
    rhs_round = rhs_full.astype(jnp.bfloat16)
    start = jnp.einsum("ncb,mnbd->nmcd", rhs_round, inverse, preferred_element_type=jnp.float32)
    iterate = start.reshape(dev_rows, 2 * col_count, -1)
    for sweep_step in range(SWEEPS):
        rounded = iterate.astype(jnp.bfloat16)
        with_e, with_a = apply_pair(fetch_halo(rounded), slot_index, e_mats, a_mats)
        e_real, e_imag = with_e[:, :col_count], with_e[:, col_count:]
        applied_real = node_real * e_real - node_imag * e_imag - with_a[:, :col_count]
        applied_imag = node_real * e_imag + node_imag * e_real - with_a[:, col_count:]
        residual = jnp.concatenate([rhs_full - applied_real, -applied_imag], axis=1).astype(jnp.bfloat16)
        products = jnp.einsum("ncb,mnbd->nmcd", residual, inverse, preferred_element_type=jnp.float32)
        products = products.reshape(dev_rows, 2, 2, col_count, -1)
        update_real = products[:, 0, 0] - products[:, 1, 1]
        update_imag = products[:, 1, 0] + products[:, 0, 1]
        iterate = iterate + jnp.concatenate([update_real, update_imag], axis=1)
    node_index = lax.axis_index("node")
    parts = iterate.reshape(dev_rows, 2, node_count, col_count // node_count, -1)
    it_real, it_imag = parts[:, 0], parts[:, 1]
    weighted = jnp.stack(
        [
            node_real * it_real - node_imag * it_imag,
            node_real * it_imag + node_imag * it_real,
        ]
    )
    weighted = jnp.transpose(weighted / node_count, (2, 0, 3, 1, 4))
    groups = node_count // 2
    core = node_index % 2
    group = node_index // 2
    paired = weighted.reshape((groups, 2) + weighted.shape[1:])
    keep = lax.dynamic_index_in_dim(paired, core, 1, keepdims=False)
    other = lax.dynamic_index_in_dim(paired, 1 - core, 1, keepdims=False)
    partial = keep + lax.ppermute(other, "node", [(j, j ^ 1) for j in range(node_count)])
    total = lax.dynamic_index_in_dim(partial, group, 0, keepdims=False)
    for offset in range(1, groups):
        chunk = lax.dynamic_index_in_dim(partial, (group + offset) % groups, 0, keepdims=False)
        perm = [(j, ((j // 2 + offset) % groups) * 2 + j % 2) for j in range(node_count)]
        total = total + lax.ppermute(chunk, "node", perm)
    return total


def solution(mesh):
    placed = (
        P(None, "rows", None),
        P("rows", None, None, None),
        P("rows", None, None, None),
        P("node", None, "rows", None, None),
        P("rows", None),
    )
    return jax.shard_map(
        per_device,
        mesh=mesh,
        in_specs=placed,
        out_specs=P(None, "node", "rows", None),
        check_vma=False,
    )
```

```python
import math

import jax
import jax.numpy as jnp
from jax import lax
from jax.sharding import PartitionSpec as P

SLOTS = 5
HMAX = 6
REACH = 2
SWEEPS = 2


def partner_offsets(peer_count):
    found = []
    for offset in list(range(1, REACH + 1)) + [peer_count // 2] + [-o for o in range(1, REACH + 1)]:
        offset = offset % peer_count
        if offset != 0 and offset not in found:
            found.append(offset)
    return found


def apply_pair(extended, slot_index, first, second):
    picked = extended[slot_index]
    with_first = jnp.einsum("nscb,nsbd->ncd", picked, first, preferred_element_type=jnp.float32)
    if second is None:
        return with_first, None
    with_second = jnp.einsum("nscb,nsbd->ncd", picked, second, preferred_element_type=jnp.float32)
    return with_first, with_second


def per_device(columns, pencil_e, pencil_a, precond, neighbours):
    dev_rows = pencil_e.shape[0]
    col_count = columns.shape[0]
    peer_count = lax.axis_size("rows")
    my_index = lax.axis_index("rows")
    offsets = partner_offsets(peer_count)
    owners = neighbours // dev_rows
    local_ids = neighbours - owners * dev_rows
    relative = (owners - my_index) % peer_count
    flat_rel = relative.reshape(-1)
    flat_local = local_ids.reshape(-1)
    slot_flat = flat_local
    wanted = []
    rank_range = jnp.arange(HMAX)
    for which, offset in enumerate(offsets):
        hit = flat_rel == offset
        rank = jnp.cumsum(hit.astype(jnp.int32)) - 1
        slot_flat = jnp.where(hit, dev_rows + which * HMAX + rank, slot_flat)
        matched = hit[None, :] & (rank[None, :] == rank_range[:, None])
        wanted.append(jnp.sum(jnp.where(matched, flat_local[None, :], 0), axis=1))
    slot_index = slot_flat.reshape(dev_rows, SLOTS)

    def to_partner(offset):
        return [(j, (j + offset) % peer_count) for j in range(peer_count)]

    def from_partner(offset):
        return [((j + offset) % peer_count, j) for j in range(peer_count)]

    asked_for = [
        lax.ppermute(wanted[which], "rows", to_partner(offset)) for which, offset in enumerate(offsets)
    ]

    def fetch_halo(vector):
        pieces = [vector]
        for which, offset in enumerate(offsets):
            pieces.append(lax.ppermute(vector[asked_for[which]], "rows", from_partner(offset)))
        return jnp.concatenate(pieces, axis=0)

    e_mats = pencil_e
    a_mats = pencil_a
    cols_major = jnp.transpose(columns, (1, 0, 2))
    rhs_full, _ = apply_pair(fetch_halo(cols_major), slot_index, e_mats, None)
    node_count = lax.axis_size("node")
    angle_node = 2.0 * math.pi * (lax.axis_index("node").astype(jnp.float32) + 0.5) / node_count
    node_real = jnp.cos(angle_node)
    node_imag = jnp.sin(angle_node)
    inverse = precond[0]
    rhs_round = rhs_full.astype(jnp.bfloat16)
    start = jnp.einsum("ncb,mnbd->nmcd", rhs_round, inverse, preferred_element_type=jnp.float32)
    iterate = start.reshape(dev_rows, 2 * col_count, -1)
    for sweep_step in range(SWEEPS):
        rounded = iterate.astype(jnp.bfloat16)
        with_e, with_a = apply_pair(fetch_halo(rounded), slot_index, e_mats, a_mats)
        e_real, e_imag = with_e[:, :col_count], with_e[:, col_count:]
        applied_real = node_real * e_real - node_imag * e_imag - with_a[:, :col_count]
        applied_imag = node_real * e_imag + node_imag * e_real - with_a[:, col_count:]
        residual = jnp.concatenate([rhs_full - applied_real, -applied_imag], axis=1).astype(jnp.bfloat16)
        products = jnp.einsum("ncb,mnbd->nmcd", residual, inverse, preferred_element_type=jnp.float32)
        products = products.reshape(dev_rows, 2, 2, col_count, -1)
        update_real = products[:, 0, 0] - products[:, 1, 1]
        update_imag = products[:, 1, 0] + products[:, 0, 1]
        iterate = iterate + jnp.concatenate([update_real, update_imag], axis=1)
    node_index = lax.axis_index("node")
    parts = iterate.reshape(dev_rows, 2, node_count, col_count // node_count, -1)
    it_real, it_imag = parts[:, 0], parts[:, 1]
    weighted = jnp.stack(
        [
            node_real * it_real - node_imag * it_imag,
            node_real * it_imag + node_imag * it_real,
        ]
    )
    weighted = jnp.transpose(weighted / node_count, (2, 0, 3, 1, 4))
    groups = node_count // 2
    core = node_index % 2
    group = node_index // 2
    paired = weighted.reshape((groups, 2) + weighted.shape[1:])
    keep = lax.dynamic_index_in_dim(paired, core, 1, keepdims=False)
    other = lax.dynamic_index_in_dim(paired, 1 - core, 1, keepdims=False)
    partial = keep + lax.ppermute(other, "node", [(j, j ^ 1) for j in range(node_count)])
    total = lax.dynamic_index_in_dim(partial, group, 0, keepdims=False)
    for offset in range(1, groups):
        chunk = lax.dynamic_index_in_dim(partial, (group + offset) % groups, 0, keepdims=False)
        perm = [(j, ((j // 2 + offset) % groups) * 2 + j % 2) for j in range(node_count)]
        total = total + lax.ppermute(chunk, "node", perm)
    return total


def solution(mesh):
    placed = (
        P(None, "rows", None),
        P("rows", None, None, None),
        P("rows", None, None, None),
        P("node", None, "rows", None, None),
        P("rows", None),
    )
    return jax.shard_map(
        per_device,
        mesh=mesh,
        in_specs=placed,
        out_specs=P(None, "node", "rows", None),
        check_vma=False,
    )
```

```python
import math

import jax
import jax.numpy as jnp
from jax import lax
from jax.sharding import PartitionSpec as P

SLOTS = 5
HMAX = 6
REACH = 2
SWEEPS = 2


def partner_offsets(peer_count):
    found = []
    order = [peer_count // 2] + [sign * o for o in range(1, REACH + 1) for sign in (1, -1)]
    for offset in order:
        offset = offset % peer_count
        if offset != 0 and offset not in found:
            found.append(offset)
    return found


def apply_pair(extended, slot_index, first, second):
    picked = extended[slot_index]
    with_first = jnp.einsum("nscb,nsbd->ncd", picked, first, preferred_element_type=jnp.float32)
    if second is None:
        return with_first, None
    with_second = jnp.einsum("nscb,nsbd->ncd", picked, second, preferred_element_type=jnp.float32)
    return with_first, with_second


def per_device(columns, pencil_e, pencil_a, precond, neighbours):
    dev_rows = pencil_e.shape[0]
    col_count = columns.shape[0]
    peer_count = lax.axis_size("rows")
    my_index = lax.axis_index("rows")
    offsets = partner_offsets(peer_count)
    owners = neighbours // dev_rows
    local_ids = neighbours - owners * dev_rows
    relative = (owners - my_index) % peer_count
    flat_rel = relative.reshape(-1)
    flat_local = local_ids.reshape(-1)
    slot_flat = flat_local
    wanted = []
    rank_range = jnp.arange(HMAX)
    for which, offset in enumerate(offsets):
        hit = flat_rel == offset
        rank = jnp.cumsum(hit.astype(jnp.int32)) - 1
        slot_flat = jnp.where(hit, dev_rows + which * HMAX + rank, slot_flat)
        matched = hit[None, :] & (rank[None, :] == rank_range[:, None])
        wanted.append(jnp.sum(jnp.where(matched, flat_local[None, :], 0), axis=1))
    slot_index = slot_flat.reshape(dev_rows, SLOTS)

    def to_partner(offset):
        return [(j, (j + offset) % peer_count) for j in range(peer_count)]

    def from_partner(offset):
        return [((j + offset) % peer_count, j) for j in range(peer_count)]

    asked_for = [
        lax.ppermute(wanted[which], "rows", to_partner(offset)) for which, offset in enumerate(offsets)
    ]

    def fetch_halo(vector):
        pieces = [vector]
        for which, offset in enumerate(offsets):
            pieces.append(lax.ppermute(vector[asked_for[which]], "rows", from_partner(offset)))
        return jnp.concatenate(pieces, axis=0)

    e_mats = pencil_e
    a_mats = pencil_a
    cols_major = jnp.transpose(columns, (1, 0, 2))
    rhs_full, _ = apply_pair(fetch_halo(cols_major), slot_index, e_mats, None)
    node_count = lax.axis_size("node")
    angle_node = 2.0 * math.pi * (lax.axis_index("node").astype(jnp.float32) + 0.5) / node_count
    node_real = jnp.cos(angle_node)
    node_imag = jnp.sin(angle_node)
    inverse = precond[0]
    rhs_round = rhs_full.astype(jnp.bfloat16)
    start = jnp.einsum("ncb,mnbd->nmcd", rhs_round, inverse, preferred_element_type=jnp.float32)
    iterate = start.reshape(dev_rows, 2 * col_count, -1)
    for sweep_step in range(SWEEPS):
        rounded = iterate.astype(jnp.bfloat16)
        with_e, with_a = apply_pair(fetch_halo(rounded), slot_index, e_mats, a_mats)
        e_real, e_imag = with_e[:, :col_count], with_e[:, col_count:]
        applied_real = node_real * e_real - node_imag * e_imag - with_a[:, :col_count]
        applied_imag = node_real * e_imag + node_imag * e_real - with_a[:, col_count:]
        residual = jnp.concatenate([rhs_full - applied_real, -applied_imag], axis=1).astype(jnp.bfloat16)
        products = jnp.einsum("ncb,mnbd->nmcd", residual, inverse, preferred_element_type=jnp.float32)
        products = products.reshape(dev_rows, 2, 2, col_count, -1)
        update_real = products[:, 0, 0] - products[:, 1, 1]
        update_imag = products[:, 1, 0] + products[:, 0, 1]
        iterate = iterate + jnp.concatenate([update_real, update_imag], axis=1)
    node_index = lax.axis_index("node")
    parts = iterate.reshape(dev_rows, 2, node_count, col_count // node_count, -1)
    it_real, it_imag = parts[:, 0], parts[:, 1]
    weighted = jnp.stack(
        [
            node_real * it_real - node_imag * it_imag,
            node_real * it_imag + node_imag * it_real,
        ]
    )
    weighted = jnp.transpose(weighted / node_count, (2, 0, 3, 1, 4))
    groups = node_count // 2
    core = node_index % 2
    group = node_index // 2
    paired = weighted.reshape((groups, 2) + weighted.shape[1:])
    keep = lax.dynamic_index_in_dim(paired, core, 1, keepdims=False)
    other = lax.dynamic_index_in_dim(paired, 1 - core, 1, keepdims=False)
    partial = keep + lax.ppermute(other, "node", [(j, j ^ 1) for j in range(node_count)])
    total = lax.dynamic_index_in_dim(partial, group, 0, keepdims=False)
    for offset in range(1, groups):
        chunk = lax.dynamic_index_in_dim(partial, (group + offset) % groups, 0, keepdims=False)
        perm = [(j, ((j // 2 + offset) % groups) * 2 + j % 2) for j in range(node_count)]
        total = total + lax.ppermute(chunk, "node", perm)
    return total


def solution(mesh):
    placed = (
        P(None, "rows", None),
        P("rows", None, None, None),
        P("rows", None, None, None),
        P("node", None, "rows", None, None),
        P("rows", None),
    )
    return jax.shard_map(
        per_device,
        mesh=mesh,
        in_specs=placed,
        out_specs=P(None, "node", "rows", None),
        check_vma=False,
    )
```

```python
import math

import jax
import jax.numpy as jnp
from jax import lax
from jax.sharding import PartitionSpec as P

SLOTS = 5
HMAX = 6
REACH = 2
SWEEPS = 2


def partner_offsets(peer_count):
    found = []
    order = [sign * o for o in range(1, REACH + 1) for sign in (1, -1)] + [peer_count // 2]
    for offset in order:
        offset = offset % peer_count
        if offset != 0 and offset not in found:
            found.append(offset)
    return found


def apply_pair(extended, slot_index, first, second):
    picked = extended[slot_index]
    with_first = jnp.einsum("nscb,nsbd->ncd", picked, first, preferred_element_type=jnp.float32)
    if second is None:
        return with_first, None
    with_second = jnp.einsum("nscb,nsbd->ncd", picked, second, preferred_element_type=jnp.float32)
    return with_first, with_second


def per_device(columns, pencil_e, pencil_a, precond, neighbours):
    dev_rows = pencil_e.shape[0]
    col_count = columns.shape[0]
    peer_count = lax.axis_size("rows")
    my_index = lax.axis_index("rows")
    offsets = partner_offsets(peer_count)
    owners = neighbours // dev_rows
    local_ids = neighbours - owners * dev_rows
    relative = (owners - my_index) % peer_count
    flat_rel = relative.reshape(-1)
    flat_local = local_ids.reshape(-1)
    slot_flat = flat_local
    wanted = []
    rank_range = jnp.arange(HMAX)
    for which, offset in enumerate(offsets):
        hit = flat_rel == offset
        rank = jnp.cumsum(hit.astype(jnp.int32)) - 1
        slot_flat = jnp.where(hit, dev_rows + which * HMAX + rank, slot_flat)
        matched = hit[None, :] & (rank[None, :] == rank_range[:, None])
        wanted.append(jnp.sum(jnp.where(matched, flat_local[None, :], 0), axis=1))
    slot_index = slot_flat.reshape(dev_rows, SLOTS)

    def to_partner(offset):
        return [(j, (j + offset) % peer_count) for j in range(peer_count)]

    def from_partner(offset):
        return [((j + offset) % peer_count, j) for j in range(peer_count)]

    asked_for = [
        lax.ppermute(wanted[which], "rows", to_partner(offset)) for which, offset in enumerate(offsets)
    ]

    def fetch_halo(vector):
        pieces = [vector]
        for which, offset in enumerate(offsets):
            pieces.append(lax.ppermute(vector[asked_for[which]], "rows", from_partner(offset)))
        return jnp.concatenate(pieces, axis=0)

    e_mats = pencil_e
    a_mats = pencil_a
    cols_major = jnp.transpose(columns, (1, 0, 2))
    rhs_full, _ = apply_pair(fetch_halo(cols_major), slot_index, e_mats, None)
    node_count = lax.axis_size("node")
    angle_node = 2.0 * math.pi * (lax.axis_index("node").astype(jnp.float32) + 0.5) / node_count
    node_real = jnp.cos(angle_node)
    node_imag = jnp.sin(angle_node)
    inverse = precond[0]
    rhs_round = rhs_full.astype(jnp.bfloat16)
    start = jnp.einsum("ncb,mnbd->nmcd", rhs_round, inverse, preferred_element_type=jnp.float32)
    iterate = start.reshape(dev_rows, 2 * col_count, -1)
    for sweep_step in range(SWEEPS):
        rounded = iterate.astype(jnp.bfloat16)
        with_e, with_a = apply_pair(fetch_halo(rounded), slot_index, e_mats, a_mats)
        e_real, e_imag = with_e[:, :col_count], with_e[:, col_count:]
        applied_real = node_real * e_real - node_imag * e_imag - with_a[:, :col_count]
        applied_imag = node_real * e_imag + node_imag * e_real - with_a[:, col_count:]
        residual = jnp.concatenate([rhs_full - applied_real, -applied_imag], axis=1).astype(jnp.bfloat16)
        products = jnp.einsum("ncb,mnbd->nmcd", residual, inverse, preferred_element_type=jnp.float32)
        products = products.reshape(dev_rows, 2, 2, col_count, -1)
        update_real = products[:, 0, 0] - products[:, 1, 1]
        update_imag = products[:, 1, 0] + products[:, 0, 1]
        iterate = iterate + jnp.concatenate([update_real, update_imag], axis=1)
    node_index = lax.axis_index("node")
    parts = iterate.reshape(dev_rows, 2, node_count, col_count // node_count, -1)
    it_real, it_imag = parts[:, 0], parts[:, 1]
    weighted = jnp.stack(
        [
            node_real * it_real - node_imag * it_imag,
            node_real * it_imag + node_imag * it_real,
        ]
    )
    weighted = jnp.transpose(weighted / node_count, (2, 0, 3, 1, 4))
    groups = node_count // 2
    core = node_index % 2
    group = node_index // 2
    paired = weighted.reshape((groups, 2) + weighted.shape[1:])
    keep = lax.dynamic_index_in_dim(paired, core, 1, keepdims=False)
    other = lax.dynamic_index_in_dim(paired, 1 - core, 1, keepdims=False)
    partial = keep + lax.ppermute(other, "node", [(j, j ^ 1) for j in range(node_count)])
    total = lax.dynamic_index_in_dim(partial, group, 0, keepdims=False)
    for offset in range(1, groups):
        chunk = lax.dynamic_index_in_dim(partial, (group + offset) % groups, 0, keepdims=False)
        perm = [(j, ((j // 2 + offset) % groups) * 2 + j % 2) for j in range(node_count)]
        total = total + lax.ppermute(chunk, "node", perm)
    return total


def solution(mesh):
    placed = (
        P(None, "rows", None),
        P("rows", None, None, None),
        P("rows", None, None, None),
        P("node", None, "rows", None, None),
        P("rows", None),
    )
    return jax.shard_map(
        per_device,
        mesh=mesh,
        in_specs=placed,
        out_specs=P(None, "node", "rows", None),
        check_vma=False,
    )
```

```python
import math

import jax
import jax.numpy as jnp
from jax import lax
from jax.sharding import PartitionSpec as P

SLOTS = 5
HMAX = 6
REACH = 2
SWEEPS = 2


def partner_offsets(peer_count):
    found = []
    for offset in list(range(1, REACH + 1)) + [peer_count // 2] + [-o for o in range(1, REACH + 1)]:
        offset = offset % peer_count
        if offset != 0 and offset not in found:
            found.append(offset)
    return found


def apply_pair(extended, slot_index, first, second):
    picked = extended[slot_index]
    with_first = jnp.einsum("nscb,nsbd->ncd", picked, first, preferred_element_type=jnp.float32)
    if second is None:
        return with_first, None
    with_second = jnp.einsum("nscb,nsbd->ncd", picked, second, preferred_element_type=jnp.float32)
    return with_first, with_second


def per_device(columns, pencil_e, pencil_a, precond, neighbours):
    dev_rows = pencil_e.shape[0]
    col_count = columns.shape[0]
    peer_count = lax.axis_size("rows")
    my_index = lax.axis_index("rows")
    offsets = partner_offsets(peer_count)
    owners = neighbours // dev_rows
    local_ids = neighbours - owners * dev_rows
    relative = (owners - my_index) % peer_count
    flat_rel = relative.reshape(-1)
    flat_local = local_ids.reshape(-1)
    slot_flat = flat_local
    wanted = []
    rank_range = jnp.arange(HMAX)
    for which, offset in enumerate(offsets):
        hit = flat_rel == offset
        rank = jnp.cumsum(hit.astype(jnp.int32)) - 1
        slot_flat = jnp.where(hit, dev_rows + which * HMAX + rank, slot_flat)
        matched = hit[None, :] & (rank[None, :] == rank_range[:, None])
        wanted.append(jnp.sum(jnp.where(matched, flat_local[None, :], 0), axis=1))
    slot_index = slot_flat.reshape(dev_rows, SLOTS)

    def to_partner(offset):
        return [(j, (j + offset) % peer_count) for j in range(peer_count)]

    def from_partner(offset):
        return [((j + offset) % peer_count, j) for j in range(peer_count)]

    asked_for = [
        lax.ppermute(wanted[which], "rows", to_partner(offset)) for which, offset in enumerate(offsets)
    ]

    def fetch_halo(vector):
        pieces = [vector]
        for which, offset in enumerate(offsets):
            pieces.append(lax.ppermute(vector[asked_for[which]], "rows", from_partner(offset)))
        return jnp.concatenate(pieces, axis=0)

    e_mats = pencil_e
    a_mats = pencil_a
    cols_major = jnp.transpose(columns, (1, 0, 2))
    rhs_full, _ = apply_pair(fetch_halo(cols_major), slot_index, e_mats, None)
    node_count = lax.axis_size("node")
    angle_node = 2.0 * math.pi * (lax.axis_index("node").astype(jnp.float32) + 0.5) / node_count
    node_real = jnp.cos(angle_node)
    node_imag = jnp.sin(angle_node)
    inverse = precond[0]
    rhs_round = rhs_full.astype(jnp.bfloat16)
    start = jnp.einsum("ncb,mnbd->nmcd", rhs_round, inverse, preferred_element_type=jnp.float32)
    iterate = start.reshape(dev_rows, 2 * col_count, -1)
    for sweep_step in range(SWEEPS):
        rounded = iterate.astype(jnp.bfloat16)
        with_e, with_a = apply_pair(fetch_halo(rounded), slot_index, e_mats, a_mats)
        e_real, e_imag = with_e[:, :col_count], with_e[:, col_count:]
        applied_real = node_real * e_real - node_imag * e_imag - with_a[:, :col_count]
        applied_imag = node_real * e_imag + node_imag * e_real - with_a[:, col_count:]
        residual = jnp.concatenate([rhs_full - applied_real, -applied_imag], axis=1).astype(jnp.bfloat16)
        products = jnp.einsum("ncb,mnbd->nmcd", residual, inverse, preferred_element_type=jnp.float32)
        products = products.reshape(dev_rows, 2, 2, col_count, -1)
        update_real = products[:, 0, 0] - products[:, 1, 1]
        update_imag = products[:, 1, 0] + products[:, 0, 1]
        iterate = iterate + jnp.concatenate([update_real, update_imag], axis=1)
    node_index = lax.axis_index("node")
    parts = iterate.reshape(dev_rows, 2, node_count, col_count // node_count, -1)
    it_real, it_imag = parts[:, 0], parts[:, 1]
    weighted = jnp.stack(
        [
            node_real * it_real - node_imag * it_imag,
            node_real * it_imag + node_imag * it_real,
        ]
    )
    weighted = jnp.transpose(weighted / node_count, (2, 0, 3, 1, 4))
    bit_count = node_count.bit_length() - 1
    data = weighted.reshape((2,) * bit_count + weighted.shape[1:])
    axis_bits = list(reversed(range(bit_count)))
    for bit in [0] + list(reversed(range(1, bit_count))):
        axis = axis_bits.index(bit)
        mine = (node_index // (2 ** bit)) % 2
        keep = lax.dynamic_index_in_dim(data, mine, axis, keepdims=False)
        other = lax.dynamic_index_in_dim(data, 1 - mine, axis, keepdims=False)
        data = keep + lax.ppermute(other, "node", [(j, j ^ (2 ** bit)) for j in range(node_count)])
        axis_bits.pop(axis)
    return data


def solution(mesh):
    placed = (
        P(None, "rows", None),
        P("rows", None, None, None),
        P("rows", None, None, None),
        P("node", None, "rows", None, None),
        P("rows", None),
    )
    return jax.shard_map(
        per_device,
        mesh=mesh,
        in_specs=placed,
        out_specs=P(None, "node", "rows", None),
        check_vma=False,
    )
```

```python
import math

import jax
import jax.numpy as jnp
from jax import lax
from jax.sharding import PartitionSpec as P

SLOTS = 5
HMAX = 6
REACH = 2
SWEEPS = 2


def partner_offsets(peer_count):
    found = []
    for offset in list(range(1, REACH + 1)) + [peer_count // 2] + [-o for o in range(1, REACH + 1)]:
        offset = offset % peer_count
        if offset != 0 and offset not in found:
            found.append(offset)
    return found


def apply_pair(extended, slot_index, first, second):
    picked = extended[slot_index]
    with_first = jnp.einsum("nscb,nsbd->ncd", picked, first, preferred_element_type=jnp.float32)
    if second is None:
        return with_first, None
    with_second = jnp.einsum("nscb,nsbd->ncd", picked, second, preferred_element_type=jnp.float32)
    return with_first, with_second


def per_device(columns, pencil_e, pencil_a, precond, neighbours):
    dev_rows = pencil_e.shape[0]
    col_count = columns.shape[0]
    peer_count = lax.axis_size("rows")
    my_index = lax.axis_index("rows")
    offsets = partner_offsets(peer_count)
    owners = neighbours // dev_rows
    local_ids = neighbours - owners * dev_rows
    relative = (owners - my_index) % peer_count
    flat_rel = relative.reshape(-1)
    flat_local = local_ids.reshape(-1)
    slot_flat = flat_local
    wanted = []
    rank_range = jnp.arange(HMAX)
    for which, offset in enumerate(offsets):
        hit = flat_rel == offset
        rank = jnp.cumsum(hit.astype(jnp.int32)) - 1
        slot_flat = jnp.where(hit, dev_rows + which * HMAX + rank, slot_flat)
        matched = hit[None, :] & (rank[None, :] == rank_range[:, None])
        wanted.append(jnp.sum(jnp.where(matched, flat_local[None, :], 0), axis=1))
    slot_index = slot_flat.reshape(dev_rows, SLOTS)

    def to_partner(offset):
        return [(j, (j + offset) % peer_count) for j in range(peer_count)]

    def from_partner(offset):
        return [((j + offset) % peer_count, j) for j in range(peer_count)]

    asked_for = [
        lax.ppermute(wanted[which], "rows", to_partner(offset)) for which, offset in enumerate(offsets)
    ]

    def fetch_halo(vector):
        pieces = [vector]
        for which, offset in enumerate(offsets):
            pieces.append(lax.ppermute(vector[asked_for[which]], "rows", from_partner(offset)))
        return jnp.concatenate(pieces, axis=0)

    e_mats = pencil_e
    both_mats = jnp.concatenate([pencil_e, pencil_a], axis=-1)
    cols_major = jnp.transpose(columns, (1, 0, 2))
    rhs_full, _ = apply_pair(fetch_halo(cols_major), slot_index, e_mats, None)
    node_count = lax.axis_size("node")
    angle_node = 2.0 * math.pi * (lax.axis_index("node").astype(jnp.float32) + 0.5) / node_count
    node_real = jnp.cos(angle_node)
    node_imag = jnp.sin(angle_node)
    inverse = precond[0]
    rhs_round = rhs_full.astype(jnp.bfloat16)
    start = jnp.einsum("ncb,mnbd->nmcd", rhs_round, inverse, preferred_element_type=jnp.float32)
    iterate = start.reshape(dev_rows, 2 * col_count, -1)
    for sweep_step in range(SWEEPS):
        rounded = iterate.astype(jnp.bfloat16)
        with_both, _ = apply_pair(fetch_halo(rounded), slot_index, both_mats, None)
        with_e, with_a = with_both[..., : pencil_e.shape[-1]], with_both[..., pencil_e.shape[-1] :]
        e_real, e_imag = with_e[:, :col_count], with_e[:, col_count:]
        applied_real = node_real * e_real - node_imag * e_imag - with_a[:, :col_count]
        applied_imag = node_real * e_imag + node_imag * e_real - with_a[:, col_count:]
        residual = jnp.concatenate([rhs_full - applied_real, -applied_imag], axis=1).astype(jnp.bfloat16)
        products = jnp.einsum("ncb,mnbd->nmcd", residual, inverse, preferred_element_type=jnp.float32)
        products = products.reshape(dev_rows, 2, 2, col_count, -1)
        update_real = products[:, 0, 0] - products[:, 1, 1]
        update_imag = products[:, 1, 0] + products[:, 0, 1]
        iterate = iterate + jnp.concatenate([update_real, update_imag], axis=1)
    node_index = lax.axis_index("node")
    parts = iterate.reshape(dev_rows, 2, node_count, col_count // node_count, -1)
    it_real, it_imag = parts[:, 0], parts[:, 1]
    weighted = jnp.stack(
        [
            node_real * it_real - node_imag * it_imag,
            node_real * it_imag + node_imag * it_real,
        ]
    )
    weighted = jnp.transpose(weighted / node_count, (2, 0, 3, 1, 4))
    groups = node_count // 2
    core = node_index % 2
    group = node_index // 2
    paired = weighted.reshape((groups, 2) + weighted.shape[1:])
    keep = lax.dynamic_index_in_dim(paired, core, 1, keepdims=False)
    other = lax.dynamic_index_in_dim(paired, 1 - core, 1, keepdims=False)
    partial = keep + lax.ppermute(other, "node", [(j, j ^ 1) for j in range(node_count)])
    total = lax.dynamic_index_in_dim(partial, group, 0, keepdims=False)
    for offset in range(1, groups):
        chunk = lax.dynamic_index_in_dim(partial, (group + offset) % groups, 0, keepdims=False)
        perm = [(j, ((j // 2 + offset) % groups) * 2 + j % 2) for j in range(node_count)]
        total = total + lax.ppermute(chunk, "node", perm)
    return total


def solution(mesh):
    placed = (
        P(None, "rows", None),
        P("rows", None, None, None),
        P("rows", None, None, None),
        P("node", None, "rows", None, None),
        P("rows", None),
    )
    return jax.shard_map(
        per_device,
        mesh=mesh,
        in_specs=placed,
        out_specs=P(None, "node", "rows", None),
        check_vma=False,
    )
```

```python
import math

import jax
import jax.numpy as jnp
from jax import lax
from jax.sharding import PartitionSpec as P

SLOTS = 5
HMAX = 6
REACH = 2
SWEEPS = 2


def partner_offsets(peer_count):
    found = []
    for offset in list(range(1, REACH + 1)) + [peer_count // 2] + [-o for o in range(1, REACH + 1)]:
        offset = offset % peer_count
        if offset != 0 and offset not in found:
            found.append(offset)
    return found


def apply_pair(extended, slot_index, first, second):
    picked = extended[slot_index]
    with_first = jnp.einsum("nscb,nsbd->ncd", picked, first, preferred_element_type=jnp.float32)
    if second is None:
        return with_first, None
    with_second = jnp.einsum("nscb,nsbd->ncd", picked, second, preferred_element_type=jnp.float32)
    return with_first, with_second


def per_device(columns, pencil_e, pencil_a, precond, neighbours):
    dev_rows = pencil_e.shape[0]
    col_count = columns.shape[0]
    peer_count = lax.axis_size("rows")
    my_index = lax.axis_index("rows")
    offsets = partner_offsets(peer_count)
    owners = neighbours // dev_rows
    local_ids = neighbours - owners * dev_rows
    relative = (owners - my_index) % peer_count
    flat_rel = relative.reshape(-1)
    flat_local = local_ids.reshape(-1)
    slot_flat = flat_local
    wanted = []
    rank_range = jnp.arange(HMAX)
    for which, offset in enumerate(offsets):
        hit = flat_rel == offset
        rank = jnp.cumsum(hit.astype(jnp.int32)) - 1
        slot_flat = jnp.where(hit, dev_rows + which * HMAX + rank, slot_flat)
        matched = hit[None, :] & (rank[None, :] == rank_range[:, None])
        wanted.append(jnp.sum(jnp.where(matched, flat_local[None, :], 0), axis=1))
    slot_index = slot_flat.reshape(dev_rows, SLOTS)

    def to_partner(offset):
        return [(j, (j + offset) % peer_count) for j in range(peer_count)]

    def from_partner(offset):
        return [((j + offset) % peer_count, j) for j in range(peer_count)]

    asked_for = [
        lax.ppermute(wanted[which], "rows", to_partner(offset)) for which, offset in enumerate(offsets)
    ]

    def fetch_halo(vector):
        pieces = [vector]
        for which, offset in enumerate(offsets):
            pieces.append(lax.ppermute(vector[asked_for[which]], "rows", from_partner(offset)))
        return jnp.concatenate(pieces, axis=0)

    e_mats = pencil_e
    a_mats = pencil_a
    cols_major = jnp.transpose(columns, (1, 0, 2))
    rhs_full, _ = apply_pair(fetch_halo(cols_major), slot_index, e_mats, None)
    node_count = lax.axis_size("node")
    angle_node = 2.0 * math.pi * (lax.axis_index("node").astype(jnp.float32) + 0.5) / node_count
    node_real = jnp.cos(angle_node)
    node_imag = jnp.sin(angle_node)
    inverse = precond[0]
    rhs_round = rhs_full.astype(jnp.bfloat16)
    start = jnp.einsum("ncb,mnbd->nmcd", rhs_round, inverse, preferred_element_type=jnp.float32)
    iterate = start.reshape(dev_rows, 2 * col_count, -1)
    for sweep_step in range(SWEEPS):
        rounded = iterate.astype(jnp.bfloat16)
        with_e, with_a = apply_pair(fetch_halo(rounded), slot_index, e_mats, a_mats)
        e_real, e_imag = with_e[:, :col_count], with_e[:, col_count:]
        applied_real = node_real * e_real - node_imag * e_imag - with_a[:, :col_count]
        applied_imag = node_real * e_imag + node_imag * e_real - with_a[:, col_count:]
        residual = jnp.concatenate([rhs_full - applied_real, -applied_imag], axis=1).astype(jnp.bfloat16)
        products = jnp.einsum("ncb,mnbd->nmcd", residual, inverse, preferred_element_type=jnp.float32)
        products = products.reshape(dev_rows, 2, 2, col_count, -1)
        update_real = products[:, 0, 0] - products[:, 1, 1]
        update_imag = products[:, 1, 0] + products[:, 0, 1]
        iterate = iterate + jnp.concatenate([update_real, update_imag], axis=1)
    node_index = lax.axis_index("node")
    parts = iterate.reshape(dev_rows, 2, node_count, col_count // node_count, -1)
    it_real, it_imag = parts[:, 0], parts[:, 1]
    weighted = jnp.stack(
        [
            node_real * it_real - node_imag * it_imag,
            node_real * it_imag + node_imag * it_real,
        ]
    )
    weighted = jnp.transpose(weighted / node_count, (2, 0, 3, 1, 4))
    groups = node_count // 2
    core = node_index % 2
    group = node_index // 2
    paired = weighted.reshape((groups, 2) + weighted.shape[1:])
    partial = lax.dynamic_index_in_dim(paired, group, 0, keepdims=False)
    for offset in range(1, groups):
        chunk = lax.dynamic_index_in_dim(paired, (group + offset) % groups, 0, keepdims=False)
        perm = [(j, ((j // 2 + offset) % groups) * 2 + j % 2) for j in range(node_count)]
        partial = partial + lax.ppermute(chunk, "node", perm)
    keep = lax.dynamic_index_in_dim(partial, core, 0, keepdims=False)
    other = lax.dynamic_index_in_dim(partial, 1 - core, 0, keepdims=False)
    return keep + lax.ppermute(other, "node", [(j, j ^ 1) for j in range(node_count)])


def solution(mesh):
    placed = (
        P(None, "rows", None),
        P("rows", None, None, None),
        P("rows", None, None, None),
        P("node", None, "rows", None, None),
        P("rows", None),
    )
    return jax.shard_map(
        per_device,
        mesh=mesh,
        in_specs=placed,
        out_specs=P(None, "node", "rows", None),
        check_vma=False,
    )
```

```python
import math

import jax
import jax.numpy as jnp
from jax import lax
from jax.sharding import PartitionSpec as P

SLOTS = 5
HMAX = 6
REACH = 2
SWEEPS = 2


def partner_offsets(peer_count):
    found = []
    for offset in list(range(1, REACH + 1)) + [peer_count // 2] + [-o for o in range(1, REACH + 1)]:
        offset = offset % peer_count
        if offset != 0 and offset not in found:
            found.append(offset)
    return found


def apply_pair(extended, slot_index, first, second):
    picked = extended[slot_index]
    with_first = jnp.einsum("nscb,nsbd->ncd", picked, first, preferred_element_type=jnp.float32)
    if second is None:
        return with_first, None
    with_second = jnp.einsum("nscb,nsbd->ncd", picked, second, preferred_element_type=jnp.float32)
    return with_first, with_second


def per_device(columns, pencil_e, pencil_a, precond, neighbours):
    dev_rows = pencil_e.shape[0]
    col_count = columns.shape[0]
    peer_count = lax.axis_size("rows")
    my_index = lax.axis_index("rows")
    offsets = partner_offsets(peer_count)
    owners = neighbours // dev_rows
    local_ids = neighbours - owners * dev_rows
    relative = (owners - my_index) % peer_count
    flat_rel = relative.reshape(-1)
    flat_local = local_ids.reshape(-1)
    slot_flat = flat_local
    wanted = []
    rank_range = jnp.arange(HMAX)
    for which, offset in enumerate(offsets):
        hit = flat_rel == offset
        rank = jnp.cumsum(hit.astype(jnp.int32)) - 1
        slot_flat = jnp.where(hit, dev_rows + which * HMAX + rank, slot_flat)
        matched = hit[None, :] & (rank[None, :] == rank_range[:, None])
        wanted.append(jnp.sum(jnp.where(matched, flat_local[None, :], 0), axis=1))
    slot_index = slot_flat.reshape(dev_rows, SLOTS)

    def to_partner(offset):
        return [(j, (j + offset) % peer_count) for j in range(peer_count)]

    def from_partner(offset):
        return [((j + offset) % peer_count, j) for j in range(peer_count)]

    asked_for = [
        lax.ppermute(wanted[which], "rows", to_partner(offset)) for which, offset in enumerate(offsets)
    ]

    asked_all = jnp.concatenate(asked_for)

    def fetch_halo(vector):
        pieces = [vector]
        outgoing = vector[asked_all]
        for which, offset in enumerate(offsets):
            piece = outgoing[which * HMAX : (which + 1) * HMAX]
            pieces.append(lax.ppermute(piece, "rows", from_partner(offset)))
        return jnp.concatenate(pieces, axis=0)

    e_mats = pencil_e
    a_mats = pencil_a
    cols_major = jnp.transpose(columns, (1, 0, 2))
    rhs_full, _ = apply_pair(fetch_halo(cols_major), slot_index, e_mats, None)
    node_count = lax.axis_size("node")
    angle_node = 2.0 * math.pi * (lax.axis_index("node").astype(jnp.float32) + 0.5) / node_count
    node_real = jnp.cos(angle_node)
    node_imag = jnp.sin(angle_node)
    inverse = precond[0]
    rhs_round = rhs_full.astype(jnp.bfloat16)
    start = jnp.einsum("ncb,mnbd->nmcd", rhs_round, inverse, preferred_element_type=jnp.float32)
    iterate = start.reshape(dev_rows, 2 * col_count, -1)
    for sweep_step in range(SWEEPS):
        rounded = iterate.astype(jnp.bfloat16)
        with_e, with_a = apply_pair(fetch_halo(rounded), slot_index, e_mats, a_mats)
        e_real, e_imag = with_e[:, :col_count], with_e[:, col_count:]
        applied_real = node_real * e_real - node_imag * e_imag - with_a[:, :col_count]
        applied_imag = node_real * e_imag + node_imag * e_real - with_a[:, col_count:]
        residual = jnp.concatenate([rhs_full - applied_real, -applied_imag], axis=1).astype(jnp.bfloat16)
        products = jnp.einsum("ncb,mnbd->nmcd", residual, inverse, preferred_element_type=jnp.float32)
        products = products.reshape(dev_rows, 2, 2, col_count, -1)
        update_real = products[:, 0, 0] - products[:, 1, 1]
        update_imag = products[:, 1, 0] + products[:, 0, 1]
        iterate = iterate + jnp.concatenate([update_real, update_imag], axis=1)
    node_index = lax.axis_index("node")
    parts = iterate.reshape(dev_rows, 2, node_count, col_count // node_count, -1)
    it_real, it_imag = parts[:, 0], parts[:, 1]
    weighted = jnp.stack(
        [
            node_real * it_real - node_imag * it_imag,
            node_real * it_imag + node_imag * it_real,
        ]
    )
    weighted = jnp.transpose(weighted / node_count, (2, 0, 3, 1, 4))
    groups = node_count // 2
    core = node_index % 2
    group = node_index // 2
    paired = weighted.reshape((groups, 2) + weighted.shape[1:])
    keep = lax.dynamic_index_in_dim(paired, core, 1, keepdims=False)
    other = lax.dynamic_index_in_dim(paired, 1 - core, 1, keepdims=False)
    partial = keep + lax.ppermute(other, "node", [(j, j ^ 1) for j in range(node_count)])
    total = lax.dynamic_index_in_dim(partial, group, 0, keepdims=False)
    for offset in range(1, groups):
        chunk = lax.dynamic_index_in_dim(partial, (group + offset) % groups, 0, keepdims=False)
        perm = [(j, ((j // 2 + offset) % groups) * 2 + j % 2) for j in range(node_count)]
        total = total + lax.ppermute(chunk, "node", perm)
    return total


def solution(mesh):
    placed = (
        P(None, "rows", None),
        P("rows", None, None, None),
        P("rows", None, None, None),
        P("node", None, "rows", None, None),
        P("rows", None),
    )
    return jax.shard_map(
        per_device,
        mesh=mesh,
        in_specs=placed,
        out_specs=P(None, "node", "rows", None),
        check_vma=False,
    )
```

```python
import math

import jax
import jax.numpy as jnp
from jax import lax
from jax.sharding import PartitionSpec as P

SLOTS = 5
HMAX = 6
REACH = 2
SWEEPS = 2


def partner_offsets(peer_count):
    found = []
    for offset in list(range(1, REACH + 1)) + [peer_count // 2] + [-o for o in range(1, REACH + 1)]:
        offset = offset % peer_count
        if offset != 0 and offset not in found:
            found.append(offset)
    return found


def apply_pair(extended, slot_index, first, second):
    picked = extended[slot_index]
    with_first = jnp.einsum("nscb,nsbd->ncd", picked, first, preferred_element_type=jnp.float32)
    if second is None:
        return with_first, None
    with_second = jnp.einsum("nscb,nsbd->ncd", picked, second, preferred_element_type=jnp.float32)
    return with_first, with_second


def per_device(columns, pencil_e, pencil_a, precond, neighbours):
    dev_rows = pencil_e.shape[0]
    col_count = columns.shape[0]
    peer_count = lax.axis_size("rows")
    my_index = lax.axis_index("rows")
    offsets = partner_offsets(peer_count)
    owners = neighbours // dev_rows
    local_ids = neighbours - owners * dev_rows
    relative = (owners - my_index) % peer_count
    flat_rel = relative.reshape(-1)
    flat_local = local_ids.reshape(-1)
    partner_ids = jnp.array(offsets, jnp.int32)
    hit = flat_rel[None, :] == partner_ids[:, None]
    rank = jnp.cumsum(hit.astype(jnp.int32), axis=1) - 1
    base = dev_rows + jnp.arange(len(offsets), dtype=jnp.int32)[:, None] * HMAX
    slot_flat = jnp.where(jnp.any(hit, axis=0), jnp.sum(jnp.where(hit, base + rank, 0), axis=0), flat_local)
    matched = hit[:, None, :] & (rank[:, None, :] == jnp.arange(HMAX)[None, :, None])
    wanted_all = jnp.sum(jnp.where(matched, flat_local[None, None, :], 0), axis=2)
    wanted = [wanted_all[which] for which in range(len(offsets))]
    slot_index = slot_flat.reshape(dev_rows, SLOTS)

    def to_partner(offset):
        return [(j, (j + offset) % peer_count) for j in range(peer_count)]

    def from_partner(offset):
        return [((j + offset) % peer_count, j) for j in range(peer_count)]

    asked_for = [
        lax.ppermute(wanted[which], "rows", to_partner(offset)) for which, offset in enumerate(offsets)
    ]

    asked_all = jnp.concatenate(asked_for)

    def fetch_halo(vector):
        pieces = [vector]
        outgoing = vector[asked_all]
        for which, offset in enumerate(offsets):
            piece = outgoing[which * HMAX : (which + 1) * HMAX]
            pieces.append(lax.ppermute(piece, "rows", from_partner(offset)))
        return jnp.concatenate(pieces, axis=0)

    e_mats = pencil_e
    a_mats = pencil_a
    cols_major = jnp.transpose(columns, (1, 0, 2))
    rhs_full, _ = apply_pair(fetch_halo(cols_major), slot_index, e_mats, None)
    node_count = lax.axis_size("node")
    angle_node = 2.0 * math.pi * (lax.axis_index("node").astype(jnp.float32) + 0.5) / node_count
    node_real = jnp.cos(angle_node)
    node_imag = jnp.sin(angle_node)
    inverse = precond[0]
    rhs_round = rhs_full.astype(jnp.bfloat16)
    start = jnp.einsum("ncb,mnbd->nmcd", rhs_round, inverse, preferred_element_type=jnp.float32)
    iterate = start.reshape(dev_rows, 2 * col_count, -1)
    for sweep_step in range(SWEEPS):
        rounded = iterate.astype(jnp.bfloat16)
        with_e, with_a = apply_pair(fetch_halo(rounded), slot_index, e_mats, a_mats)
        e_real, e_imag = with_e[:, :col_count], with_e[:, col_count:]
        applied_real = node_real * e_real - node_imag * e_imag - with_a[:, :col_count]
        applied_imag = node_real * e_imag + node_imag * e_real - with_a[:, col_count:]
        residual = jnp.concatenate([rhs_full - applied_real, -applied_imag], axis=1).astype(jnp.bfloat16)
        products = jnp.einsum("ncb,mnbd->nmcd", residual, inverse, preferred_element_type=jnp.float32)
        products = products.reshape(dev_rows, 2, 2, col_count, -1)
        update_real = products[:, 0, 0] - products[:, 1, 1]
        update_imag = products[:, 1, 0] + products[:, 0, 1]
        iterate = iterate + jnp.concatenate([update_real, update_imag], axis=1)
    node_index = lax.axis_index("node")
    parts = iterate.reshape(dev_rows, 2, node_count, col_count // node_count, -1)
    it_real, it_imag = parts[:, 0], parts[:, 1]
    weighted = jnp.stack(
        [
            node_real * it_real - node_imag * it_imag,
            node_real * it_imag + node_imag * it_real,
        ]
    )
    weighted = jnp.transpose(weighted / node_count, (2, 0, 3, 1, 4))
    groups = node_count // 2
    core = node_index % 2
    group = node_index // 2
    paired = weighted.reshape((groups, 2) + weighted.shape[1:])
    keep = lax.dynamic_index_in_dim(paired, core, 1, keepdims=False)
    other = lax.dynamic_index_in_dim(paired, 1 - core, 1, keepdims=False)
    partial = keep + lax.ppermute(other, "node", [(j, j ^ 1) for j in range(node_count)])
    total = lax.dynamic_index_in_dim(partial, group, 0, keepdims=False)
    for offset in range(1, groups):
        chunk = lax.dynamic_index_in_dim(partial, (group + offset) % groups, 0, keepdims=False)
        perm = [(j, ((j // 2 + offset) % groups) * 2 + j % 2) for j in range(node_count)]
        total = total + lax.ppermute(chunk, "node", perm)
    return total


def solution(mesh):
    placed = (
        P(None, "rows", None),
        P("rows", None, None, None),
        P("rows", None, None, None),
        P("node", None, "rows", None, None),
        P("rows", None),
    )
    return jax.shard_map(
        per_device,
        mesh=mesh,
        in_specs=placed,
        out_specs=P(None, "node", "rows", None),
        check_vma=False,
    )
```
